512 devices in a mesh: ctx: 32 (over x, y, core), head: 16 (over z).
Axes of the slice: x: 4, y: 4, z: 16, core: 2. Of those that a mesh axis runs over, the one named last changes fastest.
Arguments:
- q_linear: bfloat16 [8192, 8192], P('ctx', 'head'), may hold values from -4 to 4
- k_linear: bfloat16 [8192, 8192], P('ctx', 'head'), may hold values from -4 to 4
- v_linear: bfloat16 [8192, 8192], P('ctx', 'head'), may hold values from -40 to 40
- log_decay: float32 [8192, 64], P('ctx', 'head'), may hold values from -1 to 0
- norm_gain: float32 [8192], P('head'), may hold values from 0.5 to 1.5
- q_soft: bfloat16 [8192, 8192], P('ctx', 'head'), may hold values from -6 to 6
- k_soft: bfloat16 [8192, 1024], P('ctx'), may hold values from -4 to 4
- v_soft: bfloat16 [8192, 1024], P('ctx'), may hold values from -4 to 4
Outputs:
- linear_out: bfloat16 [8192, 8192], P('ctx', 'head')
- soft_out: bfloat16 [8192, 8192], P('ctx', 'head')
The draws below stay inside these ranges and needn't reach their ends.
All inputs are finite; a program needn't handle non-finite values.
Results may differ from the reference program's by a relative error of at most 0.0075.
Values may be sent and summed in bfloat16 or wider, within the bound.
No kernel may reach another device: no remote copies, remote signals or barrier semaphores. Data moves between devices by JAX's collectives and lax.ppermute only.
A program may use at most 64 MiB of HBM per device.

```python
import math
import jax
import jax.numpy as jnp
from jax import lax

QUERY_HEADS = 64
DH = 128
KV_HEADS = 8
BLOCK = 256
TOK_DEV = 256
SEQUENCE_TOKENS = 8192


def head_kinds(key):
    key_kind = jax.random.fold_in(key, 17)
    fast_share = 0.2
    middle_share = 0.3
    kind_draw = jax.random.uniform(key_kind, (QUERY_HEADS,), jnp.float32)
    is_fast = kind_draw < fast_share
    is_middle = jnp.logical_and(kind_draw >= fast_share, kind_draw < fast_share + middle_share)
    return (is_fast, is_middle)


def draw_v_linear(key, part):
    key_noise = jax.random.fold_in(jax.random.fold_in(key, 11), 0)
    key_row = jax.random.fold_in(jax.random.fold_in(key, 11), 1)
    key_loud = jax.random.fold_in(jax.random.fold_in(key, 11), 3)
    col_count = QUERY_HEADS * DH
    block_count = SEQUENCE_TOKENS // BLOCK
    is_fast, is_middle = head_kinds(key)
    head_factor = jnp.where(jnp.logical_or(is_fast, is_middle), 1.0, 0.02)
    head_factor = jnp.repeat(head_factor, DH)
    col_scale = 0.1 * jnp.power(10.0, jnp.arange(col_count, dtype=jnp.float32) / (col_count - 1))
    row_scale = jnp.power(10.0, jax.random.uniform(key_row, (SEQUENCE_TOKENS, 1), jnp.float32))
    loud = jax.random.randint(key_loud, (block_count,), 0, 4) == 0
    loud = jnp.logical_or(loud, jnp.arange(block_count) == 0)
    block_level = jnp.repeat(jnp.where(loud, 1.0, 0.01), BLOCK)[:, None]
    noise = jnp.clip(jax.random.normal(key_noise, (SEQUENCE_TOKENS, col_count), jnp.float32), -4.0, 4.0)
    return (noise * col_scale[None, :] * head_factor[None, :] * row_scale * block_level).astype(jnp.bfloat16)


def draw_log_decay(key, part):
    key_quick, key_middle, key_slow, key_block, key_location, key_penalty = jax.random.split(jax.random.fold_in(key, 5), 6)
    is_fast, is_middle = head_kinds(key)
    quick_rate = jax.random.uniform(key_quick, (QUERY_HEADS,), jnp.float32, minval=1.0 / 50, maxval=1.0 / 30)
    middle_rate = jax.random.uniform(key_middle, (QUERY_HEADS,), jnp.float32, minval=1.2, maxval=1.5) / BLOCK
    slow_rate = jax.random.uniform(key_slow, (QUERY_HEADS,), jnp.float32, minval=0.1, maxval=0.4) / SEQUENCE_TOKENS
    base_rate = jnp.where(is_fast, quick_rate, jnp.where(is_middle, middle_rate, slow_rate))
    block_count = SEQUENCE_TOKENS // TOK_DEV
    block_factor = jnp.exp(jax.random.uniform(key_block, (block_count, 1, QUERY_HEADS), jnp.float32, minval=0.0, maxval=math.log(2.5)))
    block_factor = jnp.broadcast_to(block_factor, (block_count, TOK_DEV, QUERY_HEADS)).reshape(SEQUENCE_TOKENS, QUERY_HEADS)
    baseline_logarithm = -base_rate[None, :] * block_factor
    spike_row_picks = jax.random.randint(key_location, (3,), 0, SEQUENCE_TOKENS)
    spike_penalty = jax.random.uniform(key_penalty, (3, QUERY_HEADS), jnp.float32, minval=0.2, maxval=0.35)
    row_identifiers = jnp.arange(SEQUENCE_TOKENS)[:, None]
    spike_logarithm = jnp.zeros((SEQUENCE_TOKENS, QUERY_HEADS), jnp.float32)
    for total_number in range(3):
        spike_logarithm = spike_logarithm + jnp.where(row_identifiers == spike_row_picks[total_number], jnp.log(1.0 - spike_penalty[total_number])[None, :], 0.0)
    return (baseline_logarithm + spike_logarithm).astype(jnp.float32)


def soft_pair(key):
    key_query = jax.random.fold_in(jax.random.fold_in(key, 3), 0)
    key_keys = jax.random.fold_in(jax.random.fold_in(key, 3), 1)
    key_places = jax.random.fold_in(jax.random.fold_in(key, 3), 4)
    key_signs = jax.random.fold_in(jax.random.fold_in(key, 3), 5)
    col_count = QUERY_HEADS * DH
    key_width = KV_HEADS * DH
    queries = jnp.clip(jax.random.normal(key_query, (SEQUENCE_TOKENS, col_count), jnp.float32), -4.0, 4.0)
    key_rows = jnp.clip(jax.random.normal(key_keys, (SEQUENCE_TOKENS, key_width), jnp.float32), -4.0, 4.0)
    row_identifiers = jnp.arange(SEQUENCE_TOKENS)[:, None]
    loud_places = jax.random.randint(key_places, (16,), 0, SEQUENCE_TOKENS)
    loud_signs = jnp.where(jax.random.normal(key_signs, (16, col_count), jnp.float32) >= 0.0, 6.0, -6.0)
    for loud_number in range(16):
        queries = jnp.where(row_identifiers == loud_places[loud_number], loud_signs[loud_number][None, :], queries)
    return (queries, key_rows)


def draw_q_soft(key, part):
    return soft_pair(key)[0].astype(jnp.bfloat16)


def draw_k_soft(key, part):
    return soft_pair(key)[1].astype(jnp.bfloat16)


def levels(key, dims, cuts, least, largest):
    def one(position, shards_of):
        heights = jax.random.uniform(jax.random.fold_in(jax.random.fold_in(key, 6), position), (shards_of,), jnp.float32, least / len(cuts), largest / len(cuts))
        return jnp.repeat(jnp.exp(heights), dims[position] // shards_of).reshape((-1,) + (1,) * (len(dims) - position - 1))

    loudness = one(*cuts[0])
    for cut in cuts[1:]:
        loudness = loudness * one(*cut)
    return loudness


def normal_values(key, shape, spread, most, shards=(), held_as=jnp.bfloat16):
    array = spread * jax.random.normal(key, shape, jnp.float32)
    if shards:
        array = array * levels(key, shape, shards, -0.22, 0.18)
    return jnp.clip(array, -most, most).astype(held_as)


def setup_inputs(seed: int = 0) -> dict:
    streams_of = jax.random.split(jax.random.key(seed), 9)
    return {
        "q_linear": normal_values(streams_of[0], (SEQUENCE_TOKENS, QUERY_HEADS * DH), 1.0, 4.0, ((0, 32), (1, 16))),
        "k_linear": normal_values(streams_of[1], (SEQUENCE_TOKENS, QUERY_HEADS * DH), 1.0, 4.0, ((0, 32), (1, 16))),
        "v_linear": draw_v_linear(jax.random.fold_in(streams_of[8], 71), 0),
        "log_decay": draw_log_decay(jax.random.fold_in(streams_of[8], 71), 0),
        "norm_gain": jnp.clip(1.0 + 0.1 * jax.random.normal(streams_of[4], (QUERY_HEADS * DH,), jnp.float32), 0.5, 1.5),
        "q_soft": draw_q_soft(jax.random.fold_in(streams_of[8], 71), 0),
        "k_soft": draw_k_soft(jax.random.fold_in(streams_of[8], 71), 0),
        "v_soft": normal_values(streams_of[7], (SEQUENCE_TOKENS, KV_HEADS * DH), 1.0, 4.0, ((0, 32),)),
    }


EPSILON = 1e-06
NEGATIVE = -1e+30

def lightning_block(running, inputs):
    queries, key_rows, value_rows, log_gates = inputs
    row_count = queries.shape[0]
    cumulative = jnp.cumsum(log_gates, axis=0)
    final_log = cumulative[-1]
    positions = jnp.arange(row_count, dtype=jnp.int32)
    causal = positions[None, :] <= positions[:, None]
    cum_heads = cumulative.T
    log_gap = jnp.where(causal[None], cum_heads[:, :, None] - cum_heads[:, None, :], NEGATIVE)
    scores = jnp.einsum('thd,shd->hts', queries.astype(jnp.float32), key_rows.astype(jnp.float32))
    weights = (scores * jnp.exp(log_gap)).astype(jnp.bfloat16)
    weights = lax.optimization_barrier(weights)
    intra_part = jnp.einsum('hts,she->the', weights.astype(jnp.float32), value_rows.astype(jnp.float32))
    lifted = queries.astype(jnp.float32) * jnp.exp(cumulative)[:, :, None]
    carried = jnp.einsum('thd,hde->the', lifted, running, precision=lax.Precision.HIGHEST)
    scaled = (key_rows.astype(jnp.float32) * jnp.exp(final_log[None, :] - cumulative)[:, :, None]).astype(jnp.bfloat16)
    scaled = lax.optimization_barrier(scaled)
    block_state = jnp.einsum('shd,she->hde', scaled.astype(jnp.float32), value_rows.astype(jnp.float32))
    running = jnp.exp(final_log)[:, None, None] * running + block_state
    return (running, intra_part + carried)

def soft_update(running, queries, query_pos, key_rows, value_rows, key_pos):
    row_max, row_total, weighted = running
    scores = jnp.einsum('thd,shd->hts', queries.astype(jnp.float32), key_rows.astype(jnp.float32)) * DH ** (-0.5)
    allowed = key_pos[None, :] <= query_pos[:, None]
    scores = jnp.where(allowed[None], scores, NEGATIVE)
    new_max = jnp.maximum(row_max, lax.optimization_barrier(jnp.max(scores, axis=2)))
    probabilities = jnp.where(allowed[None], jnp.exp(scores - new_max[:, :, None]), 0.0)
    rescale = jnp.exp(row_max - new_max)
    row_total = row_total * rescale + lax.optimization_barrier(jnp.sum(probabilities, axis=2))
    rounded = lax.optimization_barrier(probabilities.astype(jnp.bfloat16))
    weighted = weighted * rescale[:, :, None] + jnp.einsum('hts,she->hte', rounded.astype(jnp.float32), value_rows.astype(jnp.float32))
    return (new_max, row_total, weighted)

def reference(q_linear, k_linear, v_linear, log_decay, norm_gain, q_soft, k_soft, v_soft):
    block_count = SEQUENCE_TOKENS // BLOCK
    lin_shape = (block_count, BLOCK, QUERY_HEADS, DH)
    sequences = (q_linear.reshape(lin_shape), k_linear.reshape(lin_shape), v_linear.reshape(lin_shape), log_decay.reshape(block_count, BLOCK, QUERY_HEADS))
    initial = jnp.zeros((QUERY_HEADS, DH, DH), jnp.float32)
    _, mixed = lax.scan(lightning_block, initial, sequences)
    mixed = mixed.reshape(SEQUENCE_TOKENS, QUERY_HEADS * DH)
    power = lax.optimization_barrier(jnp.mean(mixed * mixed, axis=1, keepdims=True))
    linear_out = (mixed * lax.rsqrt(power + EPSILON) * norm_gain.astype(jnp.float32)[None, :]).astype(jnp.bfloat16)
    query_count = SEQUENCE_TOKENS // TOK_DEV
    group_size = QUERY_HEADS // KV_HEADS
    query_blocks = q_soft.reshape(query_count, TOK_DEV, QUERY_HEADS, DH)
    key_blocks = k_soft.reshape(query_count, TOK_DEV, KV_HEADS, DH)
    value_blocks = v_soft.reshape(query_count, TOK_DEV, KV_HEADS, DH)
    positions = jnp.arange(TOK_DEV, dtype=jnp.int32)
    block_ids = jnp.arange(query_count, dtype=jnp.int32)

    def one_query(inputs):
        queries, block_index = inputs
        query_pos = block_index * TOK_DEV + positions
        initial_soft = (jnp.full((QUERY_HEADS, TOK_DEV), NEGATIVE, jnp.float32), jnp.zeros((QUERY_HEADS, TOK_DEV), jnp.float32), jnp.zeros((QUERY_HEADS, TOK_DEV, DH), jnp.float32))

        def over_keys(running, other):
            key_rows, value_rows, key_index = other
            wide_keys = jnp.repeat(key_rows, group_size, axis=1)
            wide_values = jnp.repeat(value_rows, group_size, axis=1)
            updated = lax.cond(key_index <= block_index, lambda state: soft_update(state, queries, query_pos, wide_keys, wide_values, key_index * TOK_DEV + positions), lambda state: state, running)
            return (updated, None)
        (row_max, row_total, weighted), _ = lax.scan(over_keys, initial_soft, (key_blocks, value_blocks, block_ids))
        return jnp.transpose(weighted / row_total[:, :, None], (1, 0, 2))
    attended = lax.map(one_query, (query_blocks, block_ids))
    soft_out = attended.reshape(SEQUENCE_TOKENS, QUERY_HEADS * DH).astype(jnp.bfloat16)
    return (linear_out, soft_out)
```

```python
import functools

import jax
import jax.numpy as jnp
from jax import lax
from jax.experimental import pallas as pl
from jax.experimental.pallas import tpu as pltpu
from jax.sharding import PartitionSpec as P

QUERY_HEADS = 64
DH = 128
KV_HEADS = 8
BLOCK = 256
KEY_BLOCK = 256


EPSILON = 1e-06
NEGATIVE = -1e30


def shifted(value, axis, steps):
    count = lax.axis_size(axis)
    first, last = (max(0, -steps), min(count, count - steps))
    return lax.ppermute(value, axis, [(source, source + steps) for source in range(first, last)])


def lightning_step(carry, inputs):
    running, log_before = carry
    queries, key_rows, value_rows, log_gates = inputs
    row_count = queries.shape[0]
    cumulative = jnp.cumsum(log_gates, axis=0)
    final_log = cumulative[-1]
    positions = jnp.arange(row_count, dtype=jnp.int32)
    causal = positions[None, :] <= positions[:, None]
    cum_heads = cumulative.T
    log_gap = jnp.where(causal[None], cum_heads[:, :, None] - cum_heads[:, None, :], NEGATIVE)
    scores = jnp.einsum("thd,shd->hts", queries, key_rows, preferred_element_type=jnp.float32)
    weights = (scores * jnp.exp(log_gap)).astype(jnp.bfloat16)
    intra_part = jnp.einsum("hts,she->the", weights, value_rows, preferred_element_type=jnp.float32)
    query_wide = queries.astype(jnp.float32)
    lifted_here = query_wide * jnp.exp(cumulative)[:, :, None]
    carried_here = jnp.einsum("thd,hde->the", lifted_here, running, precision=lax.Precision.HIGHEST)
    lifted_device = query_wide * jnp.exp(cumulative + log_before[None, :])[:, :, None]
    scaled = (key_rows * jnp.exp(final_log[None, :] - cumulative)[:, :, None]).astype(jnp.bfloat16)
    block_state = jnp.einsum("shd,she->hde", scaled, value_rows, preferred_element_type=jnp.float32)
    running = jnp.exp(final_log)[:, None, None] * running + block_state
    return ((running, log_before + final_log), (intra_part + carried_here, lifted_device))


def exclusive_scan(log_total, block_state, axis):
    log_acc, state_acc = shifted((log_total, block_state), axis, 1)
    count = lax.axis_size(axis)
    step = 1
    while step < count:
        log_in, state_in = shifted((log_acc, state_acc), axis, step)
        state_acc = jnp.exp(log_acc)[:, None, None] * state_in + state_acc
        log_acc = log_acc + log_in
        step *= 2
    return state_acc


def soft_kernel(index_ref, q_ref, kv_ref, o_ref, max_ref, total_ref, acc_ref):
    my_index = index_ref[0]
    row_count = q_ref.shape[0]
    head_count = q_ref.shape[1] // DH
    max_ref[...] = jnp.full(max_ref.shape, NEGATIVE, jnp.float32)
    total_ref[...] = jnp.zeros(total_ref.shape, jnp.float32)
    acc_ref[...] = jnp.zeros(acc_ref.shape, jnp.float32)
    query_pos = my_index * row_count + lax.broadcasted_iota(jnp.int32, (row_count, KEY_BLOCK), 0)
    block_count = (my_index * row_count + row_count - 1) // KEY_BLOCK + 1

    def body(block, carry):
        start = pl.multiple_of(block * KEY_BLOCK, KEY_BLOCK)
        keys = kv_ref[pl.ds(start, KEY_BLOCK), 0:DH]
        values = kv_ref[pl.ds(start, KEY_BLOCK), DH : 2 * DH]
        key_pos = start + lax.broadcasted_iota(jnp.int32, (row_count, KEY_BLOCK), 1)
        allowed = key_pos <= query_pos
        for head in range(head_count):
            queries = q_ref[:, head * DH : (head + 1) * DH]
            scores = lax.dot_general(
                queries, keys, (((1,), (1,)), ((), ())), preferred_element_type=jnp.float32
            ) * DH ** (-0.5)
            scores = jnp.where(allowed, scores, NEGATIVE)
            row_max = max_ref[head]
            new_max = jnp.maximum(row_max, jnp.max(scores, axis=1, keepdims=True))
            probabilities = jnp.where(allowed, jnp.exp(scores - new_max), 0.0)
            rescale = jnp.exp(row_max - new_max)
            total_ref[head] = total_ref[head] * rescale + jnp.sum(probabilities, axis=1, keepdims=True)
            product = jnp.dot(
                probabilities.astype(jnp.bfloat16), values, preferred_element_type=jnp.float32
            )
            acc_ref[head] = acc_ref[head] * rescale + product
            max_ref[head] = new_max
        return carry

    lax.fori_loop(0, block_count, body, 0)
    for head in range(head_count):
        o_ref[:, head * DH : (head + 1) * DH] = (acc_ref[head] / total_ref[head]).astype(o_ref.dtype)


def soft_attention(my_index, queries, keys_values):
    row_count, width = queries.shape
    head_count = width // DH
    return pl.pallas_call(
        soft_kernel,
        out_shape=jax.ShapeDtypeStruct((row_count, width), jnp.bfloat16),
        in_specs=[
            pl.BlockSpec(memory_space=pltpu.SMEM),
            pl.BlockSpec(memory_space=pltpu.VMEM),
            pl.BlockSpec(memory_space=pltpu.VMEM),
        ],
        out_specs=pl.BlockSpec(memory_space=pltpu.VMEM),
        scratch_shapes=[
            pltpu.VMEM((head_count, row_count, 1), jnp.float32),
            pltpu.VMEM((head_count, row_count, 1), jnp.float32),
            pltpu.VMEM((head_count, row_count, DH), jnp.float32),
        ],
    )(my_index.reshape(1), queries, keys_values)


def local(q_linear, k_linear, v_linear, log_decay, norm_gain, q_soft, k_soft, v_soft):
    row_count = q_linear.shape[0]
    head_count = log_decay.shape[1]
    width = head_count * DH
    group_size = QUERY_HEADS // KV_HEADS
    kv_count = max(1, head_count // group_size)
    kv_start = lax.axis_index("head") * head_count // group_size
    k_local = lax.dynamic_slice_in_dim(k_soft, kv_start * DH, kv_count * DH, 1)
    v_local = lax.dynamic_slice_in_dim(v_soft, kv_start * DH, kv_count * DH, 1)
    keys_values = lax.all_gather(
        jnp.concatenate([k_local, v_local], axis=1), "ctx", axis=0, tiled=True
    )

    local_blocks = row_count // BLOCK
    lin_shape = (local_blocks, BLOCK, head_count, DH)
    sequences = (
        q_linear.reshape(lin_shape),
        k_linear.reshape(lin_shape),
        v_linear.reshape(lin_shape),
        log_decay.reshape(local_blocks, BLOCK, head_count),
    )
    start_carry = (
        jnp.zeros((head_count, DH, DH), jnp.float32),
        jnp.zeros((head_count,), jnp.float32),
    )
    (block_state, log_total), (local_part, lifted) = lax.scan(
        lightning_step, start_carry, sequences
    )
    local_part = local_part.reshape(row_count, head_count, DH)
    lifted = lifted.reshape(row_count, head_count, DH)
    entering = exclusive_scan(log_total, block_state, "ctx")
    carried = jnp.einsum("thd,hde->the", lifted, entering, precision=lax.Precision.HIGHEST)
    mixed = (local_part + carried).reshape(row_count, width)
    power = lax.psum(jnp.sum(mixed * mixed, axis=1), "head") / (QUERY_HEADS * DH)
    linear_out = (mixed * lax.rsqrt(power + EPSILON)[:, None] * norm_gain[None, :]).astype(
        jnp.bfloat16
    )

    my_index = lax.axis_index("ctx").astype(jnp.int32)
    if kv_count == 1:
        soft_out = soft_attention(my_index, q_soft, keys_values)
    else:
        raise NotImplementedError("kv_count > 1")
    return (linear_out, soft_out)


def solution(mesh):
    return jax.shard_map(
        local,
        mesh=mesh,
        in_specs=(
            P("ctx", "head"),
            P("ctx", "head"),
            P("ctx", "head"),
            P("ctx", "head"),
            P("head"),
            P("ctx", "head"),
            P("ctx", None),
            P("ctx", None),
        ),
        out_specs=(P("ctx", "head"), P("ctx", "head")),
        check_vma=False,
    )
```

```python
import functools

import jax
import jax.numpy as jnp
from jax import lax
from jax.experimental import pallas as pl
from jax.experimental.pallas import tpu as pltpu
from jax.sharding import PartitionSpec as P

QUERY_HEADS = 64
DH = 128
KV_HEADS = 8
BLOCK = 256
KEY_BLOCK = 256


EPSILON = 1e-06
NEGATIVE = -1e30


def shifted(value, axis, steps):
    count = lax.axis_size(axis)
    first, last = (max(0, -steps), min(count, count - steps))
    return lax.ppermute(value, axis, [(source, source + steps) for source in range(first, last)])


def lightning_step(carry, inputs):
    running, log_before = carry
    queries, key_rows, value_rows, log_gates = inputs
    row_count = queries.shape[0]
    cumulative = jnp.cumsum(log_gates, axis=0)
    final_log = cumulative[-1]
    positions = jnp.arange(row_count, dtype=jnp.int32)
    causal = positions[None, :] <= positions[:, None]
    cum_heads = cumulative.T
    log_gap = jnp.where(causal[None], cum_heads[:, :, None] - cum_heads[:, None, :], NEGATIVE)
    scores = jnp.einsum("thd,shd->hts", queries, key_rows, preferred_element_type=jnp.float32)
    weights = (scores * jnp.exp(log_gap)).astype(jnp.bfloat16)
    intra_part = jnp.einsum("hts,she->the", weights, value_rows, preferred_element_type=jnp.float32)
    query_wide = queries.astype(jnp.float32)
    lifted_here = query_wide * jnp.exp(cumulative)[:, :, None]
    carried_here = jnp.einsum("thd,hde->the", lifted_here, running, precision=lax.Precision.HIGHEST)
    lifted_device = query_wide * jnp.exp(cumulative + log_before[None, :])[:, :, None]
    scaled = (key_rows * jnp.exp(final_log[None, :] - cumulative)[:, :, None]).astype(jnp.bfloat16)
    block_state = jnp.einsum("shd,she->hde", scaled, value_rows, preferred_element_type=jnp.float32)
    running = jnp.exp(final_log)[:, None, None] * running + block_state
    return ((running, log_before + final_log), (intra_part + carried_here, lifted_device))


def exclusive_scan(log_total, block_state, axis):
    head_count, rows, cols = block_state.shape

    def pack(log, state):
        return jnp.concatenate(
            [state, jnp.broadcast_to(log[:, None, None], (head_count, 8, cols))], axis=1
        )

    packed = shifted(pack(log_total, block_state), axis, 1)
    count = lax.axis_size(axis)
    step = 1
    while step < count:
        incoming = shifted(packed, axis, step)
        log_acc = packed[:, rows, 0]
        state = jnp.exp(log_acc)[:, None, None] * incoming[:, :rows] + packed[:, :rows]
        packed = pack(log_acc + incoming[:, rows, 0], state)
        step *= 2
    return packed[:, :rows]


def ring_sum(value, axis):
    count = lax.axis_size(axis)
    if count & (count - 1):
        return lax.psum(value, axis)
    total = value
    step = 1
    while step < count:
        total = total + lax.ppermute(
            total, axis, [(source, (source + step) % count) for source in range(count)]
        )
        step *= 2
    return total


def soft_kernel(index_ref, q_ref, kv_ref, vt_ref, o_ref, max_ref, total_ref, acc_ref):
    my_index = index_ref[0]
    row_count = o_ref.shape[0]
    head_count = o_ref.shape[1] // DH
    wide = q_ref.shape[0]
    max_ref[...] = jnp.full(max_ref.shape, NEGATIVE, jnp.float32)
    total_ref[...] = jnp.zeros(total_ref.shape, jnp.float32)
    acc_ref[...] = jnp.zeros(acc_ref.shape, jnp.float32)
    full_blocks = (my_index * row_count) // KEY_BLOCK
    block_count = (my_index * row_count + row_count - 1) // KEY_BLOCK + 1

    def update(block, masked):
        start = pl.multiple_of(block * KEY_BLOCK, KEY_BLOCK)
        keys = kv_ref[pl.ds(start, KEY_BLOCK), 0:DH]
        values_t = vt_ref[:, pl.ds(start, KEY_BLOCK)]
        scores = lax.dot_general(
            keys, q_ref[...], (((1,), (1,)), ((), ())), preferred_element_type=jnp.float32
        ) * DH ** (-0.5)
        if masked:
            key_pos = start + lax.broadcasted_iota(jnp.int32, (KEY_BLOCK, wide), 0)
            query_pos = my_index * row_count + lax.rem(
                lax.broadcasted_iota(jnp.int32, (KEY_BLOCK, wide), 1), row_count
            )
            allowed = key_pos <= query_pos
            scores = jnp.where(allowed, scores, NEGATIVE)
        row_max = max_ref[...]
        new_max = jnp.maximum(row_max, jnp.max(scores, axis=0, keepdims=True))
        probabilities = jnp.exp(scores - new_max)
        if masked:
            probabilities = jnp.where(allowed, probabilities, 0.0)
        rescale = jnp.exp(row_max - new_max)
        total_ref[...] = total_ref[...] * rescale + jnp.sum(probabilities, axis=0, keepdims=True)
        product = jnp.dot(
            values_t, probabilities.astype(jnp.bfloat16), preferred_element_type=jnp.float32
        )
        acc_ref[...] = acc_ref[...] * rescale + product
        max_ref[...] = new_max

    def plain(block, carry):
        update(block, False)
        return carry

    def diagonal(block, carry):
        update(block, True)
        return carry

    lax.fori_loop(0, full_blocks, plain, 0)
    lax.fori_loop(full_blocks, block_count, diagonal, 0)
    for head in range(head_count):
        cols = slice(head * row_count, (head + 1) * row_count)
        ratio = acc_ref[:, cols] / total_ref[:, cols]
        o_ref[:, head * DH : (head + 1) * DH] = ratio.T.astype(o_ref.dtype)


def soft_attention(my_index, queries, keys_values):
    row_count, width = queries.shape
    head_count = width // DH
    wide = head_count * row_count
    stacked = queries.reshape(row_count, head_count, DH).transpose(1, 0, 2).reshape(wide, DH)
    values_t = keys_values[:, DH : 2 * DH].T
    return pl.pallas_call(
        soft_kernel,
        out_shape=jax.ShapeDtypeStruct((row_count, width), jnp.bfloat16),
        in_specs=[
            pl.BlockSpec(memory_space=pltpu.SMEM),
            pl.BlockSpec(memory_space=pltpu.VMEM),
            pl.BlockSpec(memory_space=pltpu.VMEM),
            pl.BlockSpec(memory_space=pltpu.VMEM),
        ],
        out_specs=pl.BlockSpec(memory_space=pltpu.VMEM),
        scratch_shapes=[
            pltpu.VMEM((1, wide), jnp.float32),
            pltpu.VMEM((1, wide), jnp.float32),
            pltpu.VMEM((DH, wide), jnp.float32),
        ],
    )(my_index.reshape(1), stacked, keys_values, values_t)


def local(q_linear, k_linear, v_linear, log_decay, norm_gain, q_soft, k_soft, v_soft):
    row_count = q_linear.shape[0]
    head_count = log_decay.shape[1]
    width = head_count * DH
    group_size = QUERY_HEADS // KV_HEADS
    kv_count = max(1, head_count // group_size)
    kv_start = lax.axis_index("head") * head_count // group_size
    k_local = lax.dynamic_slice_in_dim(k_soft, kv_start * DH, kv_count * DH, 1)
    v_local = lax.dynamic_slice_in_dim(v_soft, kv_start * DH, kv_count * DH, 1)
    keys_values = lax.all_gather(
        jnp.concatenate([k_local, v_local], axis=1), "ctx", axis=0, tiled=True
    )

    local_blocks = row_count // BLOCK
    lin_shape = (local_blocks, BLOCK, head_count, DH)
    sequences = (
        q_linear.reshape(lin_shape),
        k_linear.reshape(lin_shape),
        v_linear.reshape(lin_shape),
        log_decay.reshape(local_blocks, BLOCK, head_count),
    )
    start_carry = (
        jnp.zeros((head_count, DH, DH), jnp.float32),
        jnp.zeros((head_count,), jnp.float32),
    )
    (block_state, log_total), (local_part, lifted) = lax.scan(
        lightning_step, start_carry, sequences
    )
    local_part = local_part.reshape(row_count, head_count, DH)
    lifted = lifted.reshape(row_count, head_count, DH)
    entering = exclusive_scan(log_total, block_state, "ctx")
    carried = jnp.einsum("thd,hde->the", lifted, entering, precision=lax.Precision.HIGHEST)
    mixed = (local_part + carried).reshape(row_count, width)
    power = ring_sum(jnp.sum(mixed * mixed, axis=1), "head") / (QUERY_HEADS * DH)
    linear_out = (mixed * lax.rsqrt(power + EPSILON)[:, None] * norm_gain[None, :]).astype(
        jnp.bfloat16
    )

    my_index = lax.axis_index("ctx").astype(jnp.int32)
    if kv_count == 1:
        soft_out = soft_attention(my_index, q_soft, keys_values)
    else:
        raise NotImplementedError("kv_count > 1")
    return (linear_out, soft_out)


def solution(mesh):
    return jax.shard_map(
        local,
        mesh=mesh,
        in_specs=(
            P("ctx", "head"),
            P("ctx", "head"),
            P("ctx", "head"),
            P("ctx", "head"),
            P("head"),
            P("ctx", "head"),
            P("ctx", None),
            P("ctx", None),
        ),
        out_specs=(P("ctx", "head"), P("ctx", "head")),
        check_vma=False,
    )
```

```python
import jax
import jax.numpy as jnp
from jax import lax
from jax.experimental import pallas as pl
from jax.experimental.pallas import tpu as pltpu
from jax.sharding import PartitionSpec as P


QUERY_HEADS = 64
DH = 128
KV_HEADS = 8
BLOCK = 256
KEY_BLOCK = 256


EPSILON = 1e-06
NEGATIVE = -1e30


def shifted(value, axis, steps):
    count = lax.axis_size(axis)
    first, last = (max(0, -steps), min(count, count - steps))
    return lax.ppermute(value, axis, [(source, source + steps) for source in range(first, last)])


def lightning_step(carry, inputs):
    running, log_before = carry
    queries, key_rows, value_rows, log_gates = inputs
    row_count = queries.shape[0]
    cumulative = jnp.cumsum(log_gates, axis=0)
    final_log = cumulative[-1]
    positions = jnp.arange(row_count, dtype=jnp.int32)
    causal = positions[None, :] <= positions[:, None]
    cum_heads = cumulative.T
    log_gap = jnp.where(causal[None], cum_heads[:, :, None] - cum_heads[:, None, :], NEGATIVE)
    scores = jnp.einsum("thd,shd->hts", queries, key_rows, preferred_element_type=jnp.float32)
    weights = (scores * jnp.exp(log_gap)).astype(jnp.bfloat16)
    intra_part = jnp.einsum("hts,she->the", weights, value_rows, preferred_element_type=jnp.float32)
    query_wide = queries.astype(jnp.float32)
    lifted_here = query_wide * jnp.exp(cumulative)[:, :, None]
    carried_here = jnp.einsum("thd,hde->the", lifted_here, running, precision=lax.Precision.HIGHEST)
    lifted_device = query_wide * jnp.exp(cumulative + log_before[None, :])[:, :, None]
    scaled = (key_rows * jnp.exp(final_log[None, :] - cumulative)[:, :, None]).astype(jnp.bfloat16)
    block_state = jnp.einsum("shd,she->hde", scaled, value_rows, preferred_element_type=jnp.float32)
    running = jnp.exp(final_log)[:, None, None] * running + block_state
    return ((running, log_before + final_log), (intra_part + carried_here, lifted_device))


def exclusive_scan(log_total, block_state, axis):
    head_count, rows, cols = block_state.shape

    def pack(log, state):
        return jnp.concatenate(
            [state, jnp.broadcast_to(log[:, None, None], (head_count, 8, cols))], axis=1
        )

    count = lax.axis_size(axis)
    window_log, window_state = None, None
    step = 1
    while step < count:
        if window_log is None:
            sent_log, sent_state = log_total, block_state
        else:
            sent_state = jnp.exp(log_total)[:, None, None] * window_state + block_state
            sent_log = window_log + log_total
        incoming = shifted(pack(sent_log, sent_state), axis, step)
        incoming_log, incoming_state = incoming[:, rows, 0], incoming[:, :rows]
        if window_log is None:
            window_log, window_state = incoming_log, incoming_state
        else:
            window_state = jnp.exp(window_log)[:, None, None] * incoming_state + window_state
            window_log = window_log + incoming_log
        step *= 2
    return window_state


def all_sum(value, axis):
    count = lax.axis_size(axis)
    total = value
    for distance in range(1, count):
        total = total + lax.ppermute(
            value, axis, [(source, (source + distance) % count) for source in range(count)]
        )
    return total


def soft_kernel(index_ref, q_ref, kvt_ref, o_ref, max_ref, total_ref, acc_ref):
    my_index = index_ref[0]
    row_count = o_ref.shape[0]
    head_count = o_ref.shape[1] // DH
    wide = q_ref.shape[0]
    max_ref[...] = jnp.full(max_ref.shape, NEGATIVE, jnp.float32)
    total_ref[...] = jnp.zeros(total_ref.shape, jnp.float32)
    acc_ref[...] = jnp.zeros(acc_ref.shape, jnp.float32)
    full_blocks = (my_index * row_count) // KEY_BLOCK
    block_count = (my_index * row_count + row_count - 1) // KEY_BLOCK + 1

    def update(block, masked):
        start = pl.multiple_of(block * KEY_BLOCK, KEY_BLOCK)
        keys_t = kvt_ref[0:DH, pl.ds(start, KEY_BLOCK)]
        values_t = kvt_ref[DH : 2 * DH, pl.ds(start, KEY_BLOCK)]
        scores = lax.dot_general(
            keys_t, q_ref[...], (((0,), (1,)), ((), ())), preferred_element_type=jnp.float32
        ) * DH ** (-0.5)
        if masked:
            key_pos = start + lax.broadcasted_iota(jnp.int32, (KEY_BLOCK, wide), 0)
            query_pos = my_index * row_count + lax.rem(
                lax.broadcasted_iota(jnp.int32, (KEY_BLOCK, wide), 1), row_count
            )
            allowed = key_pos <= query_pos
            scores = jnp.where(allowed, scores, NEGATIVE)
        row_max = max_ref[...]
        new_max = jnp.maximum(row_max, jnp.max(scores, axis=0, keepdims=True))
        probabilities = jnp.exp(scores - new_max)
        if masked:
            probabilities = jnp.where(allowed, probabilities, 0.0)
        rescale = jnp.exp(row_max - new_max)
        total_ref[...] = total_ref[...] * rescale + jnp.sum(probabilities, axis=0, keepdims=True)
        product = jnp.dot(
            values_t, probabilities.astype(jnp.bfloat16), preferred_element_type=jnp.float32
        )
        acc_ref[...] = acc_ref[...] * rescale + product
        max_ref[...] = new_max

    def plain(block, carry):
        update(block, False)
        return carry

    def diagonal(block, carry):
        update(block, True)
        return carry

    lax.fori_loop(0, full_blocks, plain, 0)
    lax.fori_loop(full_blocks, block_count, diagonal, 0)
    for head in range(head_count):
        cols = slice(head * row_count, (head + 1) * row_count)
        ratio = acc_ref[:, cols] / total_ref[:, cols]
        o_ref[:, head * DH : (head + 1) * DH] = ratio.T.astype(o_ref.dtype)


def soft_attention(my_index, queries, keys_values):
    row_count, width = queries.shape
    head_count = width // DH
    wide = head_count * row_count
    stacked = queries.reshape(row_count, head_count, DH).transpose(1, 0, 2).reshape(wide, DH)
    keys_values_t = keys_values.T
    return pl.pallas_call(
        soft_kernel,
        out_shape=jax.ShapeDtypeStruct((row_count, width), jnp.bfloat16),
        in_specs=[
            pl.BlockSpec(memory_space=pltpu.SMEM),
            pl.BlockSpec(memory_space=pltpu.VMEM),
            pl.BlockSpec(memory_space=pltpu.VMEM),
        ],
        out_specs=pl.BlockSpec(memory_space=pltpu.VMEM),
        scratch_shapes=[
            pltpu.VMEM((1, wide), jnp.float32),
            pltpu.VMEM((1, wide), jnp.float32),
            pltpu.VMEM((DH, wide), jnp.float32),
        ],
    )(my_index.reshape(1), stacked, keys_values_t)


def layer(q_linear, k_linear, v_linear, log_decay, norm_gain, q_soft, k_soft, v_soft):
    row_count = q_linear.shape[0]
    head_count = log_decay.shape[1]
    width = head_count * DH
    group_size = QUERY_HEADS // KV_HEADS
    kv_count = max(1, head_count // group_size)
    kv_start = lax.axis_index("head") * head_count // group_size
    k_local = lax.dynamic_slice_in_dim(k_soft, kv_start * DH, kv_count * DH, 1)
    v_local = lax.dynamic_slice_in_dim(v_soft, kv_start * DH, kv_count * DH, 1)
    keys_values = lax.all_gather(
        jnp.concatenate([k_local, v_local], axis=1), "ctx", axis=0, tiled=True
    )

    local_blocks = row_count // BLOCK
    lin_shape = (local_blocks, BLOCK, head_count, DH)
    sequences = (
        q_linear.reshape(lin_shape),
        k_linear.reshape(lin_shape),
        v_linear.reshape(lin_shape),
        log_decay.reshape(local_blocks, BLOCK, head_count),
    )
    start_carry = (
        jnp.zeros((head_count, DH, DH), jnp.float32),
        jnp.zeros((head_count,), jnp.float32),
    )
    (block_state, log_total), (local_part, lifted) = lax.scan(
        lightning_step, start_carry, sequences
    )
    local_part = local_part.reshape(row_count, head_count, DH)
    lifted = lifted.reshape(row_count, head_count, DH)
    entering = exclusive_scan(log_total, block_state, "ctx")
    carried = jnp.einsum("thd,hde->the", lifted, entering, precision=lax.Precision.HIGHEST)
    mixed = (local_part + carried).reshape(row_count, width)
    power = all_sum(jnp.sum(mixed * mixed, axis=1), "head") / (QUERY_HEADS * DH)
    linear_out = (mixed * lax.rsqrt(power + EPSILON)[:, None] * norm_gain[None, :]).astype(
        jnp.bfloat16
    )

    my_index = lax.axis_index("ctx").astype(jnp.int32)
    if kv_count == 1:
        soft_out = soft_attention(my_index, q_soft, keys_values)
    else:
        raise NotImplementedError("kv_count > 1")
    return (linear_out, soft_out)


def solution(mesh):
    return jax.shard_map(
        layer,
        mesh=mesh,
        in_specs=(
            P("ctx", "head"),
            P("ctx", "head"),
            P("ctx", "head"),
            P("ctx", "head"),
            P("head"),
            P("ctx", "head"),
            P("ctx", None),
            P("ctx", None),
        ),
        out_specs=(P("ctx", "head"), P("ctx", "head")),
        check_vma=False,
    )
```

```python
import jax
import jax.numpy as jnp
from jax import lax
from jax.experimental import pallas as pl
from jax.experimental.pallas import tpu as pltpu
from jax.sharding import PartitionSpec as P

import numpy as np

QUERY_HEADS = 64
DH = 128
KV_HEADS = 8
BLOCK = 256
KEY_BLOCK = 512
HEAD_AXES = ("head_hi", "head_lo")


EPSILON = 1e-06
NEGATIVE = -1e30


def shifted(value, axis, steps):
    count = lax.axis_size(axis)
    first, last = (max(0, -steps), min(count, count - steps))
    return lax.ppermute(value, axis, [(source, source + steps) for source in range(first, last)])


def lightning_step(carry, inputs):
    running, log_before = carry
    queries, key_rows, value_rows, log_gates = inputs
    row_count = queries.shape[0]
    cumulative = jnp.cumsum(log_gates, axis=0)
    final_log = cumulative[-1]
    positions = jnp.arange(row_count, dtype=jnp.int32)
    causal = positions[None, :] <= positions[:, None]
    cum_heads = cumulative.T
    log_gap = jnp.where(causal[None], cum_heads[:, :, None] - cum_heads[:, None, :], NEGATIVE)
    scores = jnp.einsum("thd,shd->hts", queries, key_rows, preferred_element_type=jnp.float32)
    weights = (scores * jnp.exp(log_gap)).astype(jnp.bfloat16)
    intra_part = jnp.einsum("hts,she->the", weights, value_rows, preferred_element_type=jnp.float32)
    query_wide = queries.astype(jnp.float32)
    lifted_here = query_wide * jnp.exp(cumulative)[:, :, None]
    carried_here = jnp.einsum("thd,hde->the", lifted_here, running, precision=lax.Precision.HIGHEST)
    lifted_device = query_wide * jnp.exp(cumulative + log_before[None, :])[:, :, None]
    scaled = (key_rows * jnp.exp(final_log[None, :] - cumulative)[:, :, None]).astype(jnp.bfloat16)
    block_state = jnp.einsum("shd,she->hde", scaled, value_rows, preferred_element_type=jnp.float32)
    running = jnp.exp(final_log)[:, None, None] * running + block_state
    return ((running, log_before + final_log), (intra_part + carried_here, lifted_device))


def exclusive_scan(log_total, block_state, axis):
    head_count, rows, cols = block_state.shape

    def pack(log, state):
        return jnp.concatenate(
            [state, jnp.broadcast_to(log[:, None, None], (head_count, 8, cols))], axis=1
        )

    count = lax.axis_size(axis)
    window_log, window_state = None, None
    step = 1
    while step < count:
        if window_log is None:
            sent_log, sent_state = log_total, block_state
        else:
            sent_state = jnp.exp(log_total)[:, None, None] * window_state + block_state
            sent_log = window_log + log_total
        incoming = shifted(pack(sent_log, sent_state), axis, step)
        incoming_log, incoming_state = incoming[:, rows, 0], incoming[:, :rows]
        if window_log is None:
            window_log, window_state = incoming_log, incoming_state
        else:
            window_state = jnp.exp(window_log)[:, None, None] * incoming_state + window_state
            window_log = window_log + incoming_log
        step *= 2
    return window_state


def split_sum(value):
    partial = lax.optimization_barrier(lax.psum(value, "head_lo"))
    return lax.psum(partial, "head_hi")


def soft_kernel(index_ref, q_ref, kvt_ref, o_ref, max_ref, total_ref, acc_ref):
    my_index = index_ref[0]
    row_count = o_ref.shape[0]
    head_count = o_ref.shape[1] // DH
    wide = q_ref.shape[0]
    max_ref[...] = jnp.full(max_ref.shape, NEGATIVE, jnp.float32)
    total_ref[...] = jnp.zeros(total_ref.shape, jnp.float32)
    acc_ref[...] = jnp.zeros(acc_ref.shape, jnp.float32)
    full_blocks = (my_index * row_count) // KEY_BLOCK
    block_count = (my_index * row_count + row_count - 1) // KEY_BLOCK + 1

    def update(block, masked):
        start = pl.multiple_of(block * KEY_BLOCK, KEY_BLOCK)
        keys_t = kvt_ref[0:DH, pl.ds(start, KEY_BLOCK)]
        values_t = kvt_ref[DH : 2 * DH, pl.ds(start, KEY_BLOCK)]
        scores = lax.dot_general(
            keys_t, q_ref[...], (((0,), (1,)), ((), ())), preferred_element_type=jnp.float32
        ) * DH ** (-0.5)
        if masked:
            key_pos = start + lax.broadcasted_iota(jnp.int32, (KEY_BLOCK, wide), 0)
            query_pos = my_index * row_count + lax.rem(
                lax.broadcasted_iota(jnp.int32, (KEY_BLOCK, wide), 1), row_count
            )
            allowed = key_pos <= query_pos
            scores = jnp.where(allowed, scores, NEGATIVE)
        row_max = max_ref[...]
        new_max = jnp.maximum(row_max, jnp.max(scores, axis=0, keepdims=True))
        probabilities = jnp.exp(scores - new_max)
        if masked:
            probabilities = jnp.where(allowed, probabilities, 0.0)
        rescale = jnp.exp(row_max - new_max)
        total_ref[...] = total_ref[...] * rescale + jnp.sum(probabilities, axis=0, keepdims=True)
        product = jnp.dot(
            values_t, probabilities.astype(jnp.bfloat16), preferred_element_type=jnp.float32
        )
        acc_ref[...] = acc_ref[...] * rescale + product
        max_ref[...] = new_max

    def plain(block, carry):
        update(block, False)
        return carry

    def diagonal(block, carry):
        update(block, True)
        return carry

    lax.fori_loop(0, full_blocks, plain, 0)
    lax.fori_loop(full_blocks, block_count, diagonal, 0)
    for head in range(head_count):
        cols = slice(head * row_count, (head + 1) * row_count)
        ratio = acc_ref[:, cols] / total_ref[:, cols]
        o_ref[:, head * DH : (head + 1) * DH] = ratio.T.astype(o_ref.dtype)


def soft_attention(my_index, queries, keys_values):
    row_count, width = queries.shape
    head_count = width // DH
    wide = head_count * row_count
    stacked = queries.reshape(row_count, head_count, DH).transpose(1, 0, 2).reshape(wide, DH)
    keys_values_t = keys_values.T
    return pl.pallas_call(
        soft_kernel,
        out_shape=jax.ShapeDtypeStruct((row_count, width), jnp.bfloat16),
        in_specs=[
            pl.BlockSpec(memory_space=pltpu.SMEM),
            pl.BlockSpec(memory_space=pltpu.VMEM),
            pl.BlockSpec(memory_space=pltpu.VMEM),
        ],
        out_specs=pl.BlockSpec(memory_space=pltpu.VMEM),
        scratch_shapes=[
            pltpu.VMEM((1, wide), jnp.float32),
            pltpu.VMEM((1, wide), jnp.float32),
            pltpu.VMEM((DH, wide), jnp.float32),
        ],
    )(my_index.reshape(1), stacked, keys_values_t)


def layer(q_linear, k_linear, v_linear, log_decay, norm_gain, q_soft, k_soft, v_soft):
    row_count = q_linear.shape[0]
    head_count = log_decay.shape[1]
    width = head_count * DH
    group_size = QUERY_HEADS // KV_HEADS
    kv_count = max(1, head_count // group_size)
    kv_start = lax.axis_index(HEAD_AXES) * head_count // group_size
    k_local = lax.dynamic_slice_in_dim(k_soft, kv_start * DH, kv_count * DH, 1)
    v_local = lax.dynamic_slice_in_dim(v_soft, kv_start * DH, kv_count * DH, 1)
    keys_values = lax.all_gather(
        jnp.concatenate([k_local, v_local], axis=1), "ctx", axis=0, tiled=True
    )

    local_blocks = row_count // BLOCK
    lin_shape = (local_blocks, BLOCK, head_count, DH)
    sequences = (
        q_linear.reshape(lin_shape),
        k_linear.reshape(lin_shape),
        v_linear.reshape(lin_shape),
        log_decay.reshape(local_blocks, BLOCK, head_count),
    )
    start_carry = (
        jnp.zeros((head_count, DH, DH), jnp.float32),
        jnp.zeros((head_count,), jnp.float32),
    )
    (block_state, log_total), (local_part, lifted) = lax.scan(
        lightning_step, start_carry, sequences
    )
    local_part = local_part.reshape(row_count, head_count, DH)
    lifted = lifted.reshape(row_count, head_count, DH)
    entering = exclusive_scan(log_total, block_state, "ctx")
    carried = jnp.einsum("thd,hde->the", lifted, entering, precision=lax.Precision.HIGHEST)
    mixed = (local_part + carried).reshape(row_count, width)
    power = split_sum(jnp.sum(mixed * mixed, axis=1)) / (QUERY_HEADS * DH)
    linear_out = (mixed * lax.rsqrt(power + EPSILON)[:, None] * norm_gain[None, :]).astype(
        jnp.bfloat16
    )

    my_index = lax.axis_index("ctx").astype(jnp.int32)
    if kv_count == 1:
        soft_out = soft_attention(my_index, q_soft, keys_values)
    else:
        raise NotImplementedError("kv_count > 1")
    return (linear_out, soft_out)


def solution(mesh):
    ctx_count, head_count = mesh.devices.shape
    low = 4 if head_count % 4 == 0 else 1
    split = jax.sharding.Mesh(
        np.asarray(mesh.devices).reshape(ctx_count, head_count // low, low), ("ctx",) + HEAD_AXES
    )
    return jax.shard_map(
        layer,
        mesh=split,
        in_specs=(
            P("ctx", HEAD_AXES),
            P("ctx", HEAD_AXES),
            P("ctx", HEAD_AXES),
            P("ctx", HEAD_AXES),
            P(HEAD_AXES),
            P("ctx", HEAD_AXES),
            P("ctx", None),
            P("ctx", None),
        ),
        out_specs=(P("ctx", HEAD_AXES), P("ctx", HEAD_AXES)),
        check_vma=False,
    )
```

```python
import jax
import jax.numpy as jnp
from jax import lax
from jax.experimental import pallas as pl
from jax.experimental.pallas import tpu as pltpu
from jax.sharding import PartitionSpec as P

import numpy as np

QUERY_HEADS = 64
DH = 128
KV_HEADS = 8
BLOCK = 256
KEY_BLOCK = 512
HEAD_AXES = ("head_8", "head_4", "head_2", "head_1")


EPSILON = 1e-06
NEGATIVE = -1e30


def shifted(value, axis, steps):
    count = lax.axis_size(axis)
    first, last = (max(0, -steps), min(count, count - steps))
    return lax.ppermute(value, axis, [(source, source + steps) for source in range(first, last)])


def lightning_step(carry, inputs):
    running, log_before = carry
    queries, key_rows, value_rows, log_gates = inputs
    row_count = queries.shape[0]
    cumulative = jnp.cumsum(log_gates, axis=0)
    final_log = cumulative[-1]
    positions = jnp.arange(row_count, dtype=jnp.int32)
    causal = positions[None, :] <= positions[:, None]
    cum_heads = cumulative.T
    log_gap = jnp.where(causal[None], cum_heads[:, :, None] - cum_heads[:, None, :], NEGATIVE)
    scores = jnp.einsum("thd,shd->hts", queries, key_rows, preferred_element_type=jnp.float32)
    weights = (scores * jnp.exp(log_gap)).astype(jnp.bfloat16)
    intra_part = jnp.einsum("hts,she->the", weights, value_rows, preferred_element_type=jnp.float32)
    query_wide = queries.astype(jnp.float32)
    lifted_here = query_wide * jnp.exp(cumulative)[:, :, None]
    carried_here = jnp.einsum("thd,hde->the", lifted_here, running, precision=lax.Precision.HIGHEST)
    lifted_device = query_wide * jnp.exp(cumulative + log_before[None, :])[:, :, None]
    scaled = (key_rows * jnp.exp(final_log[None, :] - cumulative)[:, :, None]).astype(jnp.bfloat16)
    block_state = jnp.einsum("shd,she->hde", scaled, value_rows, preferred_element_type=jnp.float32)
    running = jnp.exp(final_log)[:, None, None] * running + block_state
    return ((running, log_before + final_log), (intra_part + carried_here, lifted_device))


def exclusive_scan(log_total, block_state, axis):
    head_count, rows, cols = block_state.shape

    def pack(log, state):
        return jnp.concatenate(
            [state, jnp.broadcast_to(log[:, None, None], (head_count, 8, cols))], axis=1
        )

    count = lax.axis_size(axis)
    window_log, window_state = None, None
    step = 1
    while step < count:
        if window_log is None:
            sent_log, sent_state = log_total, block_state
        else:
            sent_state = jnp.exp(log_total)[:, None, None] * window_state + block_state
            sent_log = window_log + log_total
        incoming = shifted(pack(sent_log, sent_state), axis, step)
        incoming_log, incoming_state = incoming[:, rows, 0], incoming[:, :rows]
        if window_log is None:
            window_log, window_state = incoming_log, incoming_state
        else:
            window_state = jnp.exp(window_log)[:, None, None] * incoming_state + window_state
            window_log = window_log + incoming_log
        step *= 2
    return window_state


def split_sum(value):
    for axis in reversed(HEAD_AXES):
        value = lax.psum(value, axis)
    return value


def soft_kernel(index_ref, q_ref, kvt_ref, o_ref, max_ref, total_ref, acc_ref):
    my_index = index_ref[0]
    row_count = o_ref.shape[0]
    head_count = o_ref.shape[1] // DH
    wide = q_ref.shape[0]
    max_ref[...] = jnp.full(max_ref.shape, NEGATIVE, jnp.float32)
    total_ref[...] = jnp.zeros(total_ref.shape, jnp.float32)
    acc_ref[...] = jnp.zeros(acc_ref.shape, jnp.float32)
    full_blocks = (my_index * row_count) // KEY_BLOCK
    block_count = (my_index * row_count + row_count - 1) // KEY_BLOCK + 1

    def update(block, masked):
        start = pl.multiple_of(block * KEY_BLOCK, KEY_BLOCK)
        keys_t = kvt_ref[0:DH, pl.ds(start, KEY_BLOCK)]
        values_t = kvt_ref[DH : 2 * DH, pl.ds(start, KEY_BLOCK)]
        scores = lax.dot_general(
            keys_t, q_ref[...], (((0,), (1,)), ((), ())), preferred_element_type=jnp.float32
        ) * DH ** (-0.5)
        if masked:
            key_pos = start + lax.broadcasted_iota(jnp.int32, (KEY_BLOCK, wide), 0)
            query_pos = my_index * row_count + lax.rem(
                lax.broadcasted_iota(jnp.int32, (KEY_BLOCK, wide), 1), row_count
            )
            allowed = key_pos <= query_pos
            scores = jnp.where(allowed, scores, NEGATIVE)
        row_max = max_ref[...]
        new_max = jnp.maximum(row_max, jnp.max(scores, axis=0, keepdims=True))
        probabilities = jnp.exp(scores - new_max)
        if masked:
            probabilities = jnp.where(allowed, probabilities, 0.0)
        rescale = jnp.exp(row_max - new_max)
        total_ref[...] = total_ref[...] * rescale + jnp.sum(probabilities, axis=0, keepdims=True)
        product = jnp.dot(
            values_t, probabilities.astype(jnp.bfloat16), preferred_element_type=jnp.float32
        )
        acc_ref[...] = acc_ref[...] * rescale + product
        max_ref[...] = new_max

    def plain(block, carry):
        update(block, False)
        return carry

    def diagonal(block, carry):
        update(block, True)
        return carry

    lax.fori_loop(0, full_blocks, plain, 0)
    lax.fori_loop(full_blocks, block_count, diagonal, 0)
    for head in range(head_count):
        cols = slice(head * row_count, (head + 1) * row_count)
        ratio = acc_ref[:, cols] / total_ref[:, cols]
        o_ref[:, head * DH : (head + 1) * DH] = ratio.T.astype(o_ref.dtype)


def soft_attention(my_index, queries, keys_values):
    row_count, width = queries.shape
    head_count = width // DH
    wide = head_count * row_count
    stacked = queries.reshape(row_count, head_count, DH).transpose(1, 0, 2).reshape(wide, DH)
    keys_values_t = keys_values.T
    return pl.pallas_call(
        soft_kernel,
        out_shape=jax.ShapeDtypeStruct((row_count, width), jnp.bfloat16),
        in_specs=[
            pl.BlockSpec(memory_space=pltpu.SMEM),
            pl.BlockSpec(memory_space=pltpu.VMEM),
            pl.BlockSpec(memory_space=pltpu.VMEM),
        ],
        out_specs=pl.BlockSpec(memory_space=pltpu.VMEM),
        scratch_shapes=[
            pltpu.VMEM((1, wide), jnp.float32),
            pltpu.VMEM((1, wide), jnp.float32),
            pltpu.VMEM((DH, wide), jnp.float32),
        ],
    )(my_index.reshape(1), stacked, keys_values_t)


def layer(q_linear, k_linear, v_linear, log_decay, norm_gain, q_soft, k_soft, v_soft):
    row_count = q_linear.shape[0]
    head_count = log_decay.shape[1]
    width = head_count * DH
    group_size = QUERY_HEADS // KV_HEADS
    kv_count = max(1, head_count // group_size)
    kv_start = lax.axis_index(HEAD_AXES) * head_count // group_size
    k_local = lax.dynamic_slice_in_dim(k_soft, kv_start * DH, kv_count * DH, 1)
    v_local = lax.dynamic_slice_in_dim(v_soft, kv_start * DH, kv_count * DH, 1)
    keys_values = lax.all_gather(
        jnp.concatenate([k_local, v_local], axis=1), "ctx", axis=0, tiled=True
    )

    local_blocks = row_count // BLOCK
    lin_shape = (local_blocks, BLOCK, head_count, DH)
    sequences = (
        q_linear.reshape(lin_shape),
        k_linear.reshape(lin_shape),
        v_linear.reshape(lin_shape),
        log_decay.reshape(local_blocks, BLOCK, head_count),
    )
    start_carry = (
        jnp.zeros((head_count, DH, DH), jnp.float32),
        jnp.zeros((head_count,), jnp.float32),
    )
    (block_state, log_total), (local_part, lifted) = lax.scan(
        lightning_step, start_carry, sequences
    )
    local_part = local_part.reshape(row_count, head_count, DH)
    lifted = lifted.reshape(row_count, head_count, DH)
    entering = exclusive_scan(log_total, block_state, "ctx")
    carried = jnp.einsum("thd,hde->the", lifted, entering, precision=lax.Precision.HIGHEST)
    mixed = (local_part + carried).reshape(row_count, width)
    power = split_sum(jnp.sum(mixed * mixed, axis=1)) / (QUERY_HEADS * DH)
    linear_out = (mixed * lax.rsqrt(power + EPSILON)[:, None] * norm_gain[None, :]).astype(
        jnp.bfloat16
    )

    my_index = lax.axis_index("ctx").astype(jnp.int32)
    if kv_count == 1:
        soft_out = soft_attention(my_index, q_soft, keys_values)
    else:
        raise NotImplementedError("kv_count > 1")
    return (linear_out, soft_out)


def solution(mesh):
    ctx_count, head_count = mesh.devices.shape
    assert head_count == 2 ** len(HEAD_AXES)
    split = jax.sharding.Mesh(
        np.asarray(mesh.devices).reshape((ctx_count,) + (2,) * len(HEAD_AXES)), ("ctx",) + HEAD_AXES
    )
    return jax.shard_map(
        layer,
        mesh=split,
        in_specs=(
            P("ctx", HEAD_AXES),
            P("ctx", HEAD_AXES),
            P("ctx", HEAD_AXES),
            P("ctx", HEAD_AXES),
            P(HEAD_AXES),
            P("ctx", HEAD_AXES),
            P("ctx", None),
            P("ctx", None),
        ),
        out_specs=(P("ctx", HEAD_AXES), P("ctx", HEAD_AXES)),
        check_vma=False,
    )
```

```python
import jax
import jax.numpy as jnp
from jax import lax
from jax.experimental import pallas as pl
from jax.experimental.pallas import tpu as pltpu
from jax.sharding import PartitionSpec as P

import numpy as np

QUERY_HEADS = 64
DH = 128
KV_HEADS = 8
BLOCK = 256
KEY_BLOCK = 512
HEAD_AXES = ("head_hi", "head_lo")


EPSILON = 1e-06
NEGATIVE = -1e30


def shifted(value, axis, steps):
    count = lax.axis_size(axis)
    first, last = (max(0, -steps), min(count, count - steps))
    return lax.ppermute(value, axis, [(source, source + steps) for source in range(first, last)])


def lightning_step(carry, inputs):
    running, log_before = carry
    queries, key_rows, value_rows, log_gates = inputs
    row_count = queries.shape[0]
    cumulative = jnp.cumsum(log_gates, axis=0)
    final_log = cumulative[-1]
    positions = jnp.arange(row_count, dtype=jnp.int32)
    causal = positions[None, :] <= positions[:, None]
    cum_heads = cumulative.T
    log_gap = jnp.where(causal[None], cum_heads[:, :, None] - cum_heads[:, None, :], NEGATIVE)
    scores = jnp.einsum("thd,shd->hts", queries, key_rows, preferred_element_type=jnp.float32)
    weights = (scores * jnp.exp(log_gap)).astype(jnp.bfloat16)
    intra_part = jnp.einsum("hts,she->the", weights, value_rows, preferred_element_type=jnp.float32)
    query_wide = queries.astype(jnp.float32)
    lifted_here = query_wide * jnp.exp(cumulative)[:, :, None]
    carried_here = jnp.einsum("thd,hde->the", lifted_here, running, precision=lax.Precision.HIGHEST)
    lifted_device = query_wide * jnp.exp(cumulative + log_before[None, :])[:, :, None]
    scaled = (key_rows * jnp.exp(final_log[None, :] - cumulative)[:, :, None]).astype(jnp.bfloat16)
    block_state = jnp.einsum("shd,she->hde", scaled, value_rows, preferred_element_type=jnp.float32)
    running = jnp.exp(final_log)[:, None, None] * running + block_state
    return ((running, log_before + final_log), (intra_part + carried_here, lifted_device))


def exclusive_scan(log_total, block_state, axis):
    head_count, rows, cols = block_state.shape

    def pack(log, state):
        return jnp.concatenate(
            [state, jnp.broadcast_to(log[:, None, None], (head_count, 8, cols))], axis=1
        )

    count = lax.axis_size(axis)
    window_log, window_state = None, None
    step = 1
    while step < count:
        if window_log is None:
            sent_log, sent_state = log_total, block_state
        else:
            sent_state = jnp.exp(log_total)[:, None, None] * window_state + block_state
            sent_log = window_log + log_total
        incoming = shifted(pack(sent_log, sent_state), axis, step)
        incoming_log, incoming_state = incoming[:, rows, 0], incoming[:, :rows]
        if window_log is None:
            window_log, window_state = incoming_log, incoming_state
        else:
            window_state = jnp.exp(window_log)[:, None, None] * incoming_state + window_state
            window_log = window_log + incoming_log
        step *= 2
    return window_state


def split_sum(value):
    partial = lax.optimization_barrier(lax.psum(value, "head_lo"))
    return lax.psum(partial, "head_hi")


def soft_kernel(index_ref, q_ref, kvt_ref, o_ref, max_ref, total_ref, acc_ref):
    my_index = index_ref[0]
    row_count = o_ref.shape[0]
    head_count = o_ref.shape[1] // DH
    wide = q_ref.shape[0]
    held = kvt_ref.shape[1]
    max_ref[...] = jnp.full(max_ref.shape, NEGATIVE, jnp.float32)
    total_ref[...] = jnp.zeros(total_ref.shape, jnp.float32)
    acc_ref[...] = jnp.zeros(acc_ref.shape, jnp.float32)
    needed = (my_index + 1) * row_count
    offset = needed - held
    block_count = (needed + KEY_BLOCK - 1) // KEY_BLOCK

    def update(block, masked):
        start = pl.multiple_of(held - (block_count - block) * KEY_BLOCK, KEY_BLOCK)
        keys_t = kvt_ref[0:DH, pl.ds(start, KEY_BLOCK)]
        values_t = kvt_ref[DH : 2 * DH, pl.ds(start, KEY_BLOCK)]
        scores = lax.dot_general(
            keys_t, q_ref[...], (((0,), (1,)), ((), ())), preferred_element_type=jnp.float32
        ) * DH ** (-0.5)
        if masked:
            key_pos = start + offset + lax.broadcasted_iota(jnp.int32, (KEY_BLOCK, wide), 0)
            query_pos = my_index * row_count + lax.rem(
                lax.broadcasted_iota(jnp.int32, (KEY_BLOCK, wide), 1), row_count
            )
            allowed = jnp.logical_and(key_pos >= 0, key_pos <= query_pos)
            scores = jnp.where(allowed, scores, NEGATIVE)
        row_max = max_ref[...]
        new_max = jnp.maximum(row_max, jnp.max(scores, axis=0, keepdims=True))
        probabilities = jnp.exp(scores - new_max)
        if masked:
            probabilities = jnp.where(allowed, probabilities, 0.0)
        rescale = jnp.exp(row_max - new_max)
        total_ref[...] = total_ref[...] * rescale + jnp.sum(probabilities, axis=0, keepdims=True)
        product = jnp.dot(
            values_t, probabilities.astype(jnp.bfloat16), preferred_element_type=jnp.float32
        )
        acc_ref[...] = acc_ref[...] * rescale + product
        max_ref[...] = new_max

    def plain(block, carry):
        update(block, False)
        return carry

    update(0, True)
    lax.fori_loop(1, block_count - 1, plain, 0)

    @pl.when(block_count > 1)
    def _():
        update(block_count - 1, True)

    for head in range(head_count):
        cols = slice(head * row_count, (head + 1) * row_count)
        ratio = acc_ref[:, cols] / total_ref[:, cols]
        o_ref[:, head * DH : (head + 1) * DH] = ratio.T.astype(o_ref.dtype)


def soft_attention(my_index, queries, keys_values_t):
    row_count, width = queries.shape
    head_count = width // DH
    wide = head_count * row_count
    stacked = queries.reshape(row_count, head_count, DH).transpose(1, 0, 2).reshape(wide, DH)
    return pl.pallas_call(
        soft_kernel,
        out_shape=jax.ShapeDtypeStruct((row_count, width), jnp.bfloat16),
        in_specs=[
            pl.BlockSpec(memory_space=pltpu.SMEM),
            pl.BlockSpec(memory_space=pltpu.VMEM),
            pl.BlockSpec(memory_space=pltpu.VMEM),
        ],
        out_specs=pl.BlockSpec(memory_space=pltpu.VMEM),
        scratch_shapes=[
            pltpu.VMEM((1, wide), jnp.float32),
            pltpu.VMEM((1, wide), jnp.float32),
            pltpu.VMEM((DH, wide), jnp.float32),
        ],
    )(my_index.reshape(1), stacked, keys_values_t)


def prefix_window(block, axis):
    window = block
    count = lax.axis_size(axis)
    step = 1
    while step < count:
        window = jnp.concatenate([shifted(window, axis, step), window], axis=1)
        step *= 2
    return window


def layer(q_linear, k_linear, v_linear, log_decay, norm_gain, q_soft, k_soft, v_soft):
    row_count = q_linear.shape[0]
    head_count = log_decay.shape[1]
    width = head_count * DH
    group_size = QUERY_HEADS // KV_HEADS
    kv_count = max(1, head_count // group_size)
    kv_start = lax.axis_index(HEAD_AXES) * head_count // group_size
    k_local = lax.dynamic_slice_in_dim(k_soft, kv_start * DH, kv_count * DH, 1)
    v_local = lax.dynamic_slice_in_dim(v_soft, kv_start * DH, kv_count * DH, 1)
    keys_values_t = prefix_window(jnp.concatenate([k_local, v_local], axis=1).T, "ctx")

    local_blocks = row_count // BLOCK
    lin_shape = (local_blocks, BLOCK, head_count, DH)
    sequences = (
        q_linear.reshape(lin_shape),
        k_linear.reshape(lin_shape),
        v_linear.reshape(lin_shape),
        log_decay.reshape(local_blocks, BLOCK, head_count),
    )
    start_carry = (
        jnp.zeros((head_count, DH, DH), jnp.float32),
        jnp.zeros((head_count,), jnp.float32),
    )
    (block_state, log_total), (local_part, lifted) = lax.scan(
        lightning_step, start_carry, sequences
    )
    local_part = local_part.reshape(row_count, head_count, DH)
    lifted = lifted.reshape(row_count, head_count, DH)
    entering = exclusive_scan(log_total, block_state, "ctx")
    carried = jnp.einsum("thd,hde->the", lifted, entering, precision=lax.Precision.HIGHEST)
    mixed = (local_part + carried).reshape(row_count, width)
    power = split_sum(jnp.sum(mixed * mixed, axis=1)) / (QUERY_HEADS * DH)
    linear_out = (mixed * lax.rsqrt(power + EPSILON)[:, None] * norm_gain[None, :]).astype(
        jnp.bfloat16
    )

    my_index = lax.axis_index("ctx").astype(jnp.int32)
    if kv_count == 1:
        soft_out = soft_attention(my_index, q_soft, keys_values_t)
    else:
        raise NotImplementedError("kv_count > 1")
    return (linear_out, soft_out)


def solution(mesh):
    ctx_count, head_count = mesh.devices.shape
    low = 4 if head_count % 4 == 0 else 1
    split = jax.sharding.Mesh(
        np.asarray(mesh.devices).reshape(ctx_count, head_count // low, low), ("ctx",) + HEAD_AXES
    )
    return jax.shard_map(
        layer,
        mesh=split,
        in_specs=(
            P("ctx", HEAD_AXES),
            P("ctx", HEAD_AXES),
            P("ctx", HEAD_AXES),
            P("ctx", HEAD_AXES),
            P(HEAD_AXES),
            P("ctx", HEAD_AXES),
            P("ctx", None),
            P("ctx", None),
        ),
        out_specs=(P("ctx", HEAD_AXES), P("ctx", HEAD_AXES)),
        check_vma=False,
    )
```

```python
import jax
import jax.numpy as jnp
from jax import lax
from jax.experimental import pallas as pl
from jax.experimental.pallas import tpu as pltpu
from jax.sharding import PartitionSpec as P

import numpy as np

QUERY_HEADS = 64
DH = 128
KV_HEADS = 8
BLOCK = 256
KEY_BLOCK = 512
HEAD_AXES = ("head_hi", "head_2", "head_1")


EPSILON = 1e-06
NEGATIVE = -1e30


def shifted(value, axis, steps):
    count = lax.axis_size(axis)
    first, last = (max(0, -steps), min(count, count - steps))
    return lax.ppermute(value, axis, [(source, source + steps) for source in range(first, last)])


def lightning_step(carry, inputs):
    running, log_before = carry
    queries, key_rows, value_rows, log_gates = inputs
    row_count = queries.shape[0]
    cumulative = jnp.cumsum(log_gates, axis=0)
    final_log = cumulative[-1]
    positions = jnp.arange(row_count, dtype=jnp.int32)
    causal = positions[None, :] <= positions[:, None]
    cum_heads = cumulative.T
    log_gap = jnp.where(causal[None], cum_heads[:, :, None] - cum_heads[:, None, :], NEGATIVE)
    scores = jnp.einsum("thd,shd->hts", queries, key_rows, preferred_element_type=jnp.float32)
    weights = (scores * jnp.exp(log_gap)).astype(jnp.bfloat16)
    intra_part = jnp.einsum("hts,she->the", weights, value_rows, preferred_element_type=jnp.float32)
    query_wide = queries.astype(jnp.float32)
    lifted_here = query_wide * jnp.exp(cumulative)[:, :, None]
    carried_here = jnp.einsum("thd,hde->the", lifted_here, running, precision=lax.Precision.HIGHEST)
    lifted_device = query_wide * jnp.exp(cumulative + log_before[None, :])[:, :, None]
    scaled = (key_rows * jnp.exp(final_log[None, :] - cumulative)[:, :, None]).astype(jnp.bfloat16)
    block_state = jnp.einsum("shd,she->hde", scaled, value_rows, preferred_element_type=jnp.float32)
    running = jnp.exp(final_log)[:, None, None] * running + block_state
    return ((running, log_before + final_log), (intra_part + carried_here, lifted_device))


def exclusive_scan(log_total, block_state, axis):
    head_count, rows, cols = block_state.shape

    def pack(log, state):
        return jnp.concatenate(
            [state, jnp.broadcast_to(log[:, None, None], (head_count, 8, cols))], axis=1
        )

    count = lax.axis_size(axis)
    window_log, window_state = None, None
    step = 1
    while step < count:
        if window_log is None:
            sent_log, sent_state = log_total, block_state
        else:
            sent_state = jnp.exp(log_total)[:, None, None] * window_state + block_state
            sent_log = window_log + log_total
        incoming = shifted(pack(sent_log, sent_state), axis, step)
        incoming_log, incoming_state = incoming[:, rows, 0], incoming[:, :rows]
        if window_log is None:
            window_log, window_state = incoming_log, incoming_state
        else:
            window_state = jnp.exp(window_log)[:, None, None] * incoming_state + window_state
            window_log = window_log + incoming_log
        step *= 2
    return window_state


def split_sum(value):
    for axis in reversed(HEAD_AXES):
        value = lax.psum(value, axis)
    return value


def soft_kernel(index_ref, q_ref, kvt_ref, o_ref, max_ref, total_ref, acc_ref):
    my_index = index_ref[0]
    row_count = o_ref.shape[0]
    head_count = o_ref.shape[1] // DH
    wide = q_ref.shape[0]
    max_ref[...] = jnp.full(max_ref.shape, NEGATIVE, jnp.float32)
    total_ref[...] = jnp.zeros(total_ref.shape, jnp.float32)
    acc_ref[...] = jnp.zeros(acc_ref.shape, jnp.float32)
    full_blocks = (my_index * row_count) // KEY_BLOCK
    block_count = (my_index * row_count + row_count - 1) // KEY_BLOCK + 1

    def update(block, masked):
        start = pl.multiple_of(block * KEY_BLOCK, KEY_BLOCK)
        keys_t = kvt_ref[0:DH, pl.ds(start, KEY_BLOCK)]
        values_t = kvt_ref[DH : 2 * DH, pl.ds(start, KEY_BLOCK)]
        scores = lax.dot_general(
            keys_t, q_ref[...], (((0,), (1,)), ((), ())), preferred_element_type=jnp.float32
        ) * DH ** (-0.5)
        if masked:
            key_pos = start + lax.broadcasted_iota(jnp.int32, (KEY_BLOCK, wide), 0)
            query_pos = my_index * row_count + lax.rem(
                lax.broadcasted_iota(jnp.int32, (KEY_BLOCK, wide), 1), row_count
            )
            allowed = key_pos <= query_pos
            scores = jnp.where(allowed, scores, NEGATIVE)
        row_max = max_ref[...]
        new_max = jnp.maximum(row_max, jnp.max(scores, axis=0, keepdims=True))
        probabilities = jnp.exp(scores - new_max)
        if masked:
            probabilities = jnp.where(allowed, probabilities, 0.0)
        rescale = jnp.exp(row_max - new_max)
        total_ref[...] = total_ref[...] * rescale + jnp.sum(probabilities, axis=0, keepdims=True)
        product = jnp.dot(
            values_t, probabilities.astype(jnp.bfloat16), preferred_element_type=jnp.float32
        )
        acc_ref[...] = acc_ref[...] * rescale + product
        max_ref[...] = new_max

    def plain(block, carry):
        update(block, False)
        return carry

    def diagonal(block, carry):
        update(block, True)
        return carry

    lax.fori_loop(0, full_blocks, plain, 0)
    lax.fori_loop(full_blocks, block_count, diagonal, 0)
    for head in range(head_count):
        cols = slice(head * row_count, (head + 1) * row_count)
        ratio = acc_ref[:, cols] / total_ref[:, cols]
        o_ref[:, head * DH : (head + 1) * DH] = ratio.T.astype(o_ref.dtype)


def soft_attention(my_index, queries, keys_values):
    row_count, width = queries.shape
    head_count = width // DH
    wide = head_count * row_count
    stacked = queries.reshape(row_count, head_count, DH).transpose(1, 0, 2).reshape(wide, DH)
    keys_values_t = keys_values.T
    return pl.pallas_call(
        soft_kernel,
        out_shape=jax.ShapeDtypeStruct((row_count, width), jnp.bfloat16),
        in_specs=[
            pl.BlockSpec(memory_space=pltpu.SMEM),
            pl.BlockSpec(memory_space=pltpu.VMEM),
            pl.BlockSpec(memory_space=pltpu.VMEM),
        ],
        out_specs=pl.BlockSpec(memory_space=pltpu.VMEM),
        scratch_shapes=[
            pltpu.VMEM((1, wide), jnp.float32),
            pltpu.VMEM((1, wide), jnp.float32),
            pltpu.VMEM((DH, wide), jnp.float32),
        ],
    )(my_index.reshape(1), stacked, keys_values_t)


def layer(q_linear, k_linear, v_linear, log_decay, norm_gain, q_soft, k_soft, v_soft):
    row_count = q_linear.shape[0]
    head_count = log_decay.shape[1]
    width = head_count * DH
    group_size = QUERY_HEADS // KV_HEADS
    kv_count = max(1, head_count // group_size)
    kv_start = lax.axis_index(HEAD_AXES) * head_count // group_size
    k_local = lax.dynamic_slice_in_dim(k_soft, kv_start * DH, kv_count * DH, 1)
    v_local = lax.dynamic_slice_in_dim(v_soft, kv_start * DH, kv_count * DH, 1)
    keys_values = lax.all_gather(
        jnp.concatenate([k_local, v_local], axis=1), "ctx", axis=0, tiled=True
    )

    local_blocks = row_count // BLOCK
    lin_shape = (local_blocks, BLOCK, head_count, DH)
    sequences = (
        q_linear.reshape(lin_shape),
        k_linear.reshape(lin_shape),
        v_linear.reshape(lin_shape),
        log_decay.reshape(local_blocks, BLOCK, head_count),
    )
    start_carry = (
        jnp.zeros((head_count, DH, DH), jnp.float32),
        jnp.zeros((head_count,), jnp.float32),
    )
    (block_state, log_total), (local_part, lifted) = lax.scan(
        lightning_step, start_carry, sequences
    )
    local_part = local_part.reshape(row_count, head_count, DH)
    lifted = lifted.reshape(row_count, head_count, DH)
    entering = exclusive_scan(log_total, block_state, "ctx")
    carried = jnp.einsum("thd,hde->the", lifted, entering, precision=lax.Precision.HIGHEST)
    mixed = (local_part + carried).reshape(row_count, width)
    power = split_sum(jnp.sum(mixed * mixed, axis=1)) / (QUERY_HEADS * DH)
    linear_out = (mixed * lax.rsqrt(power + EPSILON)[:, None] * norm_gain[None, :]).astype(
        jnp.bfloat16
    )

    my_index = lax.axis_index("ctx").astype(jnp.int32)
    if kv_count == 1:
        soft_out = soft_attention(my_index, q_soft, keys_values)
    else:
        raise NotImplementedError("kv_count > 1")
    return (linear_out, soft_out)


def solution(mesh):
    ctx_count, head_count = mesh.devices.shape
    split = jax.sharding.Mesh(
        np.asarray(mesh.devices).reshape(ctx_count, head_count // 4, 2, 2), ("ctx",) + HEAD_AXES
    )
    return jax.shard_map(
        layer,
        mesh=split,
        in_specs=(
            P("ctx", HEAD_AXES),
            P("ctx", HEAD_AXES),
            P("ctx", HEAD_AXES),
            P("ctx", HEAD_AXES),
            P(HEAD_AXES),
            P("ctx", HEAD_AXES),
            P("ctx", None),
            P("ctx", None),
        ),
        out_specs=(P("ctx", HEAD_AXES), P("ctx", HEAD_AXES)),
        check_vma=False,
    )
```

```python
import jax
import jax.numpy as jnp
from jax import lax
from jax.experimental import pallas as pl
from jax.experimental.pallas import tpu as pltpu
from jax.sharding import PartitionSpec as P

import numpy as np

QUERY_HEADS = 64
DH = 128
KV_HEADS = 8
BLOCK = 256
KEY_BLOCK = 1024
HEAD_AXES = ("head_hi", "head_lo")


EPSILON = 1e-06
LOG2E = 1.4426950408889634
NEGATIVE = -1e30


def shifted(value, axis, steps):
    count = lax.axis_size(axis)
    first, last = (max(0, -steps), min(count, count - steps))
    return lax.ppermute(value, axis, [(source, source + steps) for source in range(first, last)])


def lightning_step(carry, inputs):
    running, log_before = carry
    queries, key_rows, value_rows, log_gates = inputs
    row_count = queries.shape[0]
    cumulative = jnp.cumsum(log_gates, axis=0)
    final_log = cumulative[-1]
    positions = jnp.arange(row_count, dtype=jnp.int32)
    causal = positions[None, :] <= positions[:, None]
    cum_heads = cumulative.T
    log_gap = jnp.where(causal[None], cum_heads[:, :, None] - cum_heads[:, None, :], NEGATIVE)
    scores = jnp.einsum("thd,shd->hts", queries, key_rows, preferred_element_type=jnp.float32)
    weights = (scores * jnp.exp(log_gap)).astype(jnp.bfloat16)
    intra_part = jnp.einsum("hts,she->the", weights, value_rows, preferred_element_type=jnp.float32)
    query_wide = queries.astype(jnp.float32)
    lifted_here = query_wide * jnp.exp(cumulative)[:, :, None]
    carried_here = jnp.einsum("thd,hde->the", lifted_here, running, precision=lax.Precision.HIGHEST)
    lifted_device = query_wide * jnp.exp(cumulative + log_before[None, :])[:, :, None]
    scaled = (key_rows * jnp.exp(final_log[None, :] - cumulative)[:, :, None]).astype(jnp.bfloat16)
    block_state = jnp.einsum("shd,she->hde", scaled, value_rows, preferred_element_type=jnp.float32)
    running = jnp.exp(final_log)[:, None, None] * running + block_state
    return ((running, log_before + final_log), (intra_part + carried_here, lifted_device))


def exclusive_scan(log_total, block_state, axis):
    head_count, rows, cols = block_state.shape

    def pack(log, state):
        return jnp.concatenate(
            [state, jnp.broadcast_to(log[:, None, None], (head_count, 8, cols))], axis=1
        )

    count = lax.axis_size(axis)
    window_log, window_state = None, None
    step = 1
    while step < count:
        if window_log is None:
            sent_log, sent_state = log_total, block_state
        else:
            sent_state = jnp.exp(log_total)[:, None, None] * window_state + block_state
            sent_log = window_log + log_total
        incoming = shifted(pack(sent_log, sent_state), axis, step)
        incoming_log, incoming_state = incoming[:, rows, 0], incoming[:, :rows]
        if window_log is None:
            window_log, window_state = incoming_log, incoming_state
        else:
            window_state = jnp.exp(window_log)[:, None, None] * incoming_state + window_state
            window_log = window_log + incoming_log
        step *= 2
    return window_state


def split_sum(value):
    partial = lax.optimization_barrier(lax.psum(value, "head_lo"))
    return lax.psum(partial, "head_hi")


def soft_kernel(index_ref, q_ref, kvt_ref, o_ref, max_ref, total_ref, acc_ref):
    my_index = index_ref[0]
    row_count = o_ref.shape[0]
    head_count = o_ref.shape[1] // DH
    wide = q_ref.shape[0]
    max_ref[...] = jnp.full(max_ref.shape, NEGATIVE, jnp.float32)
    total_ref[...] = jnp.zeros(total_ref.shape, jnp.float32)
    acc_ref[...] = jnp.zeros(acc_ref.shape, jnp.float32)
    full_blocks = (my_index * row_count) // KEY_BLOCK
    block_count = (my_index * row_count + row_count - 1) // KEY_BLOCK + 1

    def update(block, masked):
        start = pl.multiple_of(block * KEY_BLOCK, KEY_BLOCK)
        keys_t = kvt_ref[0:DH, pl.ds(start, KEY_BLOCK)]
        values_t = kvt_ref[DH : 2 * DH, pl.ds(start, KEY_BLOCK)]
        scores = lax.dot_general(
            keys_t, q_ref[...], (((0,), (1,)), ((), ())), preferred_element_type=jnp.float32
        ) * (DH ** (-0.5) * LOG2E)
        if masked:
            key_pos = start + lax.broadcasted_iota(jnp.int32, (KEY_BLOCK, wide), 0)
            query_pos = my_index * row_count + lax.rem(
                lax.broadcasted_iota(jnp.int32, (KEY_BLOCK, wide), 1), row_count
            )
            allowed = key_pos <= query_pos
            scores = jnp.where(allowed, scores, NEGATIVE)
        row_max = max_ref[...]
        new_max = jnp.maximum(row_max, jnp.max(scores, axis=0, keepdims=True))
        probabilities = jnp.exp2(scores - new_max)
        if masked:
            probabilities = jnp.where(allowed, probabilities, 0.0)
        rescale = jnp.exp2(row_max - new_max)
        total_ref[...] = total_ref[...] * rescale + jnp.sum(probabilities, axis=0, keepdims=True)
        product = jnp.dot(
            values_t, probabilities.astype(jnp.bfloat16), preferred_element_type=jnp.float32
        )
        acc_ref[...] = acc_ref[...] * rescale + product
        max_ref[...] = new_max

    def plain(block, carry):
        update(block, False)
        return carry

    def diagonal(block, carry):
        update(block, True)
        return carry

    lax.fori_loop(0, full_blocks, plain, 0)
    lax.fori_loop(full_blocks, block_count, diagonal, 0)
    for head in range(head_count):
        cols = slice(head * row_count, (head + 1) * row_count)
        ratio = acc_ref[:, cols] / total_ref[:, cols]
        o_ref[:, head * DH : (head + 1) * DH] = ratio.T.astype(o_ref.dtype)


def soft_attention(my_index, queries, keys_values):
    row_count, width = queries.shape
    head_count = width // DH
    wide = head_count * row_count
    stacked = queries.reshape(row_count, head_count, DH).transpose(1, 0, 2).reshape(wide, DH)
    keys_values_t = keys_values.T
    return pl.pallas_call(
        soft_kernel,
        out_shape=jax.ShapeDtypeStruct((row_count, width), jnp.bfloat16),
        in_specs=[
            pl.BlockSpec(memory_space=pltpu.SMEM),
            pl.BlockSpec(memory_space=pltpu.VMEM),
            pl.BlockSpec(memory_space=pltpu.VMEM),
        ],
        out_specs=pl.BlockSpec(memory_space=pltpu.VMEM),
        scratch_shapes=[
            pltpu.VMEM((1, wide), jnp.float32),
            pltpu.VMEM((1, wide), jnp.float32),
            pltpu.VMEM((DH, wide), jnp.float32),
        ],
    )(my_index.reshape(1), stacked, keys_values_t)


def layer(q_linear, k_linear, v_linear, log_decay, norm_gain, q_soft, k_soft, v_soft):
    row_count = q_linear.shape[0]
    head_count = log_decay.shape[1]
    width = head_count * DH
    group_size = QUERY_HEADS // KV_HEADS
    kv_count = max(1, head_count // group_size)
    kv_start = lax.axis_index(HEAD_AXES) * head_count // group_size
    k_local = lax.dynamic_slice_in_dim(k_soft, kv_start * DH, kv_count * DH, 1)
    v_local = lax.dynamic_slice_in_dim(v_soft, kv_start * DH, kv_count * DH, 1)
    keys_values = lax.all_gather(
        jnp.concatenate([k_local, v_local], axis=1), "ctx", axis=0, tiled=True
    )

    local_blocks = row_count // BLOCK
    lin_shape = (local_blocks, BLOCK, head_count, DH)
    sequences = (
        q_linear.reshape(lin_shape),
        k_linear.reshape(lin_shape),
        v_linear.reshape(lin_shape),
        log_decay.reshape(local_blocks, BLOCK, head_count),
    )
    start_carry = (
        jnp.zeros((head_count, DH, DH), jnp.float32),
        jnp.zeros((head_count,), jnp.float32),
    )
    (block_state, log_total), (local_part, lifted) = lax.scan(
        lightning_step, start_carry, sequences
    )
    local_part = local_part.reshape(row_count, head_count, DH)
    lifted = lifted.reshape(row_count, head_count, DH)
    entering = exclusive_scan(log_total, block_state, "ctx")
    carried = jnp.einsum("thd,hde->the", lifted, entering, precision=lax.Precision.HIGHEST)
    mixed = (local_part + carried).reshape(row_count, width)
    power = split_sum(jnp.sum(mixed * mixed, axis=1)) / (QUERY_HEADS * DH)
    linear_out = (mixed * lax.rsqrt(power + EPSILON)[:, None] * norm_gain[None, :]).astype(
        jnp.bfloat16
    )

    my_index = lax.axis_index("ctx").astype(jnp.int32)
    if kv_count == 1:
        soft_out = soft_attention(my_index, q_soft, keys_values)
    else:
        raise NotImplementedError("kv_count > 1")
    return (linear_out, soft_out)


def solution(mesh):
    ctx_count, head_count = mesh.devices.shape
    low = 4 if head_count % 4 == 0 else 1
    split = jax.sharding.Mesh(
        np.asarray(mesh.devices).reshape(ctx_count, head_count // low, low), ("ctx",) + HEAD_AXES
    )
    return jax.shard_map(
        layer,
        mesh=split,
        in_specs=(
            P("ctx", HEAD_AXES),
            P("ctx", HEAD_AXES),
            P("ctx", HEAD_AXES),
            P("ctx", HEAD_AXES),
            P(HEAD_AXES),
            P("ctx", HEAD_AXES),
            P("ctx", None),
            P("ctx", None),
        ),
        out_specs=(P("ctx", HEAD_AXES), P("ctx", HEAD_AXES)),
        check_vma=False,
    )
```

```python
import jax
import jax.numpy as jnp
from jax import lax
from jax.experimental import pallas as pl
from jax.experimental.pallas import tpu as pltpu
from jax.sharding import PartitionSpec as P

import numpy as np

QUERY_HEADS = 64
DH = 128
KV_HEADS = 8
BLOCK = 256
KEY_BLOCK = 2048
HEAD_AXES = ("head_hi", "head_lo")


EPSILON = 1e-06
LOG2E = 1.4426950408889634
NEGATIVE = -1e30


def shifted(value, axis, steps):
    count = lax.axis_size(axis)
    first, last = (max(0, -steps), min(count, count - steps))
    return lax.ppermute(value, axis, [(source, source + steps) for source in range(first, last)])


def lightning_step(carry, inputs):
    running, log_before = carry
    queries, key_rows, value_rows, log_gates = inputs
    row_count = queries.shape[0]
    cumulative = jnp.cumsum(log_gates, axis=0)
    final_log = cumulative[-1]
    positions = jnp.arange(row_count, dtype=jnp.int32)
    causal = positions[None, :] <= positions[:, None]
    cum_heads = cumulative.T
    log_gap = jnp.where(causal[None], cum_heads[:, :, None] - cum_heads[:, None, :], NEGATIVE)
    scores = jnp.einsum("thd,shd->hts", queries, key_rows, preferred_element_type=jnp.float32)
    weights = (scores * jnp.exp(log_gap)).astype(jnp.bfloat16)
    intra_part = jnp.einsum("hts,she->the", weights, value_rows, preferred_element_type=jnp.float32)
    query_wide = queries.astype(jnp.float32)
    lifted_here = query_wide * jnp.exp(cumulative)[:, :, None]
    carried_here = jnp.einsum("thd,hde->the", lifted_here, running, precision=lax.Precision.HIGHEST)
    lifted_device = query_wide * jnp.exp(cumulative + log_before[None, :])[:, :, None]
    scaled = (key_rows * jnp.exp(final_log[None, :] - cumulative)[:, :, None]).astype(jnp.bfloat16)
    block_state = jnp.einsum("shd,she->hde", scaled, value_rows, preferred_element_type=jnp.float32)
    running = jnp.exp(final_log)[:, None, None] * running + block_state
    return ((running, log_before + final_log), (intra_part + carried_here, lifted_device))


def exclusive_scan(log_total, block_state, axis):
    head_count, rows, cols = block_state.shape
    own = jnp.concatenate(
        [block_state, jnp.broadcast_to(log_total[:, None, None], (head_count, 8, cols))], axis=1
    )
    is_state = lax.broadcasted_iota(jnp.int32, own.shape, 1) < rows

    def combine(earlier, later):
        scale = jnp.exp(later[:, rows : rows + 1, :])
        return jnp.where(is_state, scale * earlier + later, earlier + later)

    count = lax.axis_size(axis)
    window = None
    step = 1
    while step < count:
        sent = own if window is None else combine(window, own)
        incoming = shifted(sent, axis, step)
        window = incoming if window is None else combine(incoming, window)
        step *= 2
    return window[:, :rows]


def split_sum(value):
    partial = lax.optimization_barrier(lax.psum(value, "head_lo"))
    return lax.psum(partial, "head_hi")


def soft_kernel(index_ref, q_ref, kvt_ref, o_ref, max_ref, total_ref, acc_ref):
    my_index = index_ref[0]
    row_count = o_ref.shape[0]
    head_count = o_ref.shape[1] // DH
    wide = q_ref.shape[0]
    max_ref[...] = jnp.full(max_ref.shape, NEGATIVE, jnp.float32)
    total_ref[...] = jnp.zeros(total_ref.shape, jnp.float32)
    acc_ref[...] = jnp.zeros(acc_ref.shape, jnp.float32)
    full_blocks = (my_index * row_count) // KEY_BLOCK
    block_count = (my_index * row_count + row_count - 1) // KEY_BLOCK + 1

    def update(block, masked):
        start = pl.multiple_of(block * KEY_BLOCK, KEY_BLOCK)
        keys_t = kvt_ref[0:DH, pl.ds(start, KEY_BLOCK)]
        values_t = kvt_ref[DH : 2 * DH, pl.ds(start, KEY_BLOCK)]
        scores = lax.dot_general(
            keys_t, q_ref[...], (((0,), (1,)), ((), ())), preferred_element_type=jnp.float32
        ) * (DH ** (-0.5) * LOG2E)
        if masked:
            key_pos = start + lax.broadcasted_iota(jnp.int32, (KEY_BLOCK, wide), 0)
            query_pos = my_index * row_count + lax.rem(
                lax.broadcasted_iota(jnp.int32, (KEY_BLOCK, wide), 1), row_count
            )
            allowed = key_pos <= query_pos
            scores = jnp.where(allowed, scores, NEGATIVE)
        row_max = max_ref[...]
        new_max = jnp.maximum(row_max, jnp.max(scores, axis=0, keepdims=True))
        probabilities = jnp.exp2(scores - new_max)
        if masked:
            probabilities = jnp.where(allowed, probabilities, 0.0)
        rescale = jnp.exp2(row_max - new_max)
        total_ref[...] = total_ref[...] * rescale + jnp.sum(probabilities, axis=0, keepdims=True)
        product = jnp.dot(
            values_t, probabilities.astype(jnp.bfloat16), preferred_element_type=jnp.float32
        )
        acc_ref[...] = acc_ref[...] * rescale + product
        max_ref[...] = new_max

    def plain(block, carry):
        update(block, False)
        return carry

    def diagonal(block, carry):
        update(block, True)
        return carry

    lax.fori_loop(0, full_blocks, plain, 0)
    lax.fori_loop(full_blocks, block_count, diagonal, 0)
    for head in range(head_count):
        cols = slice(head * row_count, (head + 1) * row_count)
        ratio = acc_ref[:, cols] / total_ref[:, cols]
        o_ref[:, head * DH : (head + 1) * DH] = ratio.T.astype(o_ref.dtype)


def soft_attention(my_index, queries, keys_values):
    row_count, width = queries.shape
    head_count = width // DH
    wide = head_count * row_count
    stacked = queries.reshape(row_count, head_count, DH).transpose(1, 0, 2).reshape(wide, DH)
    keys_values_t = keys_values.T
    return pl.pallas_call(
        soft_kernel,
        out_shape=jax.ShapeDtypeStruct((row_count, width), jnp.bfloat16),
        in_specs=[
            pl.BlockSpec(memory_space=pltpu.SMEM),
            pl.BlockSpec(memory_space=pltpu.VMEM),
            pl.BlockSpec(memory_space=pltpu.VMEM),
        ],
        out_specs=pl.BlockSpec(memory_space=pltpu.VMEM),
        scratch_shapes=[
            pltpu.VMEM((1, wide), jnp.float32),
            pltpu.VMEM((1, wide), jnp.float32),
            pltpu.VMEM((DH, wide), jnp.float32),
        ],
    )(my_index.reshape(1), stacked, keys_values_t)


def layer(q_linear, k_linear, v_linear, log_decay, norm_gain, q_soft, k_soft, v_soft):
    row_count = q_linear.shape[0]
    head_count = log_decay.shape[1]
    width = head_count * DH
    group_size = QUERY_HEADS // KV_HEADS
    kv_count = max(1, head_count // group_size)
    kv_start = lax.axis_index(HEAD_AXES) * head_count // group_size
    k_local = lax.dynamic_slice_in_dim(k_soft, kv_start * DH, kv_count * DH, 1)
    v_local = lax.dynamic_slice_in_dim(v_soft, kv_start * DH, kv_count * DH, 1)
    keys_values = lax.all_gather(
        jnp.concatenate([k_local, v_local], axis=1), "ctx", axis=0, tiled=True
    )

    local_blocks = row_count // BLOCK
    lin_shape = (local_blocks, BLOCK, head_count, DH)
    sequences = (
        q_linear.reshape(lin_shape),
        k_linear.reshape(lin_shape),
        v_linear.reshape(lin_shape),
        log_decay.reshape(local_blocks, BLOCK, head_count),
    )
    start_carry = (
        jnp.zeros((head_count, DH, DH), jnp.float32),
        jnp.zeros((head_count,), jnp.float32),
    )
    (block_state, log_total), (local_part, lifted) = lax.scan(
        lightning_step, start_carry, sequences
    )
    local_part = local_part.reshape(row_count, head_count, DH)
    lifted = lifted.reshape(row_count, head_count, DH)
    entering = exclusive_scan(log_total, block_state, "ctx")
    carried = jnp.einsum("thd,hde->the", lifted, entering, precision=lax.Precision.HIGHEST)
    mixed = (local_part + carried).reshape(row_count, width)
    power = split_sum(jnp.sum(mixed * mixed, axis=1)) / (QUERY_HEADS * DH)
    linear_out = (mixed * lax.rsqrt(power + EPSILON)[:, None] * norm_gain[None, :]).astype(
        jnp.bfloat16
    )

    my_index = lax.axis_index("ctx").astype(jnp.int32)
    if kv_count == 1:
        soft_out = soft_attention(my_index, q_soft, keys_values)
    else:
        raise NotImplementedError("kv_count > 1")
    return (linear_out, soft_out)


def solution(mesh):
    ctx_count, head_count = mesh.devices.shape
    low = 4 if head_count % 4 == 0 else 1
    split = jax.sharding.Mesh(
        np.asarray(mesh.devices).reshape(ctx_count, head_count // low, low), ("ctx",) + HEAD_AXES
    )
    return jax.shard_map(
        layer,
        mesh=split,
        in_specs=(
            P("ctx", HEAD_AXES),
            P("ctx", HEAD_AXES),
            P("ctx", HEAD_AXES),
            P("ctx", HEAD_AXES),
            P(HEAD_AXES),
            P("ctx", HEAD_AXES),
            P("ctx", None),
            P("ctx", None),
        ),
        out_specs=(P("ctx", HEAD_AXES), P("ctx", HEAD_AXES)),
        check_vma=False,
    )
```
